256 devices in a mesh: batch: 16 (over z, core), wx: 4 (over y), wy: 4 (over x).
Axes of the slice: x: 4, y: 4, z: 8, core: 2. Of those that a mesh axis runs over, the one named last changes fastest.
Arguments:
- tokens: bfloat16 [8192, 16384], P(('batch', 'wx'), 'wy'), may hold values from -6 to 6
- routes: int32 [8192, 1], P(('batch', 'wx')), may hold values from 0 to 15; in each aligned block of 128 rows (0 to 127, 128 to 255, ...) at most 16 rows name the same one
- gate_weight: bfloat16 [16384, 2048], P('wy', 'wx'), may hold values from -0.046875 to 0.046875
- up_weight: bfloat16 [16384, 2048], P('wy', 'wx'), may hold values from -0.046875 to 0.046875
Outputs:
- hidden: bfloat16 [16384, 2048], P(('batch', 'wy'), 'wx')
The draws below stay inside these ranges and needn't reach their ends.
Inputs may be any that keep to these rules, and one draw needn't show every extreme that they name: `routes`: among the tokens of one device, at most 16 share a group.
All inputs are finite; a program needn't handle non-finite values.
Results may differ from the reference program's by a relative error of at most 0.001.
Values may be sent and summed in bfloat16 or wider, within the bound.
No kernel may reach another device: no remote copies, remote signals or barrier semaphores. Data moves between devices by JAX's collectives and lax.ppermute only.
A program may use at most 128 MiB of HBM per device.

```python
import math
import jax
import jax.numpy as jnp
import numpy as np
from jax import lax

D = 16384
ROWS_DEV = 128
HID = 2048
SLOTS = 16
GROUP_ROWS = 1024
ROWS = 8192
N_BATCH = 16
N_WX = 4


def block_levels(rng, shape, pieces, least, top_value):
    gain, own = 1.0, jax.random.fold_in(rng, 6)
    for dim, blocks in pieces:
        heights = jnp.exp(jax.random.uniform(jax.random.fold_in(own, dim), (blocks,), jnp.float32, least / len(pieces), top_value / len(pieces)))
        gain = gain * jnp.repeat(heights, shape[dim] // blocks).reshape([-1 if axis == dim else 1 for axis in range(len(shape))])
    return gain


def routed_block(rng, own, number, rows, count, top, bound, skew):
    sequence = jax.random.permutation(rng, count)
    heavy_load, usual = load_shares(count, rows * top, bound, skew, True), load_shares(count, rows * top, bound, skew, False)
    places = jnp.arange(count)

    def named(tallies, turn):
        used = int((tallies > 0).sum())
        fixed = max(1, used // 4)
        passed = fixed + (places - fixed + turn * (used - fixed)) % max(1, count - fixed)
        return jnp.zeros((count,), jnp.int32).at[sequence[jnp.where(places < fixed, places, passed)]].set(jnp.asarray(tallies, jnp.int32))

    tallies = jnp.where(number % 4 == 0, named(heavy_load, number // 4), named(usual, number - number // 4 - 1))
    mixed = jax.random.permutation(jax.random.fold_in(own, 3), count)
    giver, sink = mixed[0:count // 2 * 2:2], mixed[1:count // 2 * 2:2]
    slack = jnp.minimum(tallies[giver] - 1, bound - tallies[sink]) // 2
    slack = jnp.where((giver == sequence[0]) | (sink == sequence[0]) | (tallies[sink] == 0), 0, jnp.maximum(slack, 0))
    passed = jax.random.randint(jax.random.fold_in(own, 4), (count // 2,), 0, 1 << 20) % (slack + 1)
    tallies = tallies.at[giver].add(-passed).at[sink].add(passed)
    items = jnp.searchsorted(jnp.cumsum(tallies), jnp.arange(rows * top), side="right").astype(jnp.int32)
    table = items.reshape(top, rows).T
    table = table[jax.random.permutation(jax.random.fold_in(own, 1), rows)]
    turn = jax.random.randint(jax.random.fold_in(own, 2), (rows, 1), 0, top)
    return jnp.take_along_axis(table, (jnp.arange(top)[None, :] + turn) % top, axis=1)


def load_shares(amount, total, bound, slope, full):
    portions = [(1 << 20) // math.isqrt(grade ** slope) + 1 for grade in range(1, amount + 1)]
    largest = bound if full else min(bound, max(-(-total // amount), total * portions[0] // sum(portions)))
    least = 1 if total - largest >= amount - 1 else 0
    holding, rest = [largest] + [least] * (amount - 1), total - largest - least * (amount - 1)
    while rest > 0:
        candidates = [i for i in range(1, amount) if holding[i] < largest] or [i for i in range(1, amount) if holding[i] < bound]
        mass, budget = sum([portions[i] for i in candidates]), rest
        for i in candidates:
            extra = min(bound - holding[i], max(1, budget * portions[i] // mass), rest)
            holding[i] = holding[i] + extra
            rest = rest - extra
    return np.array(holding)


def centred(rng, extent, deviation, limit, pieces=(), kind=jnp.bfloat16):
    entries = jax.random.normal(rng, extent, jnp.float32) * deviation
    if len(pieces) > 0:
        entries = block_levels(rng, extent, pieces, -0.22, 0.18) * entries
    return jnp.clip(entries, min=-limit, max=limit).astype(kind)


def setup_inputs(seed: int = 0) -> dict:
    arg_keys = jax.random.split(jax.random.key(seed), 5)
    tokens = centred(arg_keys[0], (ROWS, D), 1.0, 6.0, ((0, 64), (1, 4)))
    routes_keys = jax.random.split(jax.random.fold_in(arg_keys[1], 1), ROWS // ROWS_DEV)
    routes_turns = jax.random.permutation(jax.random.fold_in(arg_keys[1], 3), ROWS // ROWS_DEV)
    routes = jax.vmap(lambda own, number: routed_block(jax.random.fold_in(arg_keys[1], 2), own, number, ROWS_DEV, N_BATCH, 1, SLOTS, 1))(routes_keys, routes_turns).reshape((ROWS, 1))
    gate_weight = centred(arg_keys[2], (D, HID), D ** -0.5, 0.046875, ((0, 4), (1, 4)))
    up_weight = centred(arg_keys[3], (D, HID), D ** -0.5, 0.046875, ((0, 4), (1, 4)))
    return {"tokens": tokens, "routes": routes, "gate_weight": gate_weight, "up_weight": up_weight}


def reference(tokens, routes, gate_weight, up_weight):
    blocks = N_BATCH * N_WX
    group_of = routes[:, 0].reshape(blocks, ROWS_DEV)
    onehot = (group_of[:, :, None] == jnp.arange(N_BATCH, dtype=jnp.int32)[None, None, :]).astype(jnp.int32)
    ordinal = jnp.sum((jnp.cumsum(onehot, axis=1) - onehot) * onehot, axis=2)
    source = jnp.arange(blocks, dtype=jnp.int32)
    offset = ((source % N_WX) * N_BATCH + source // N_WX) * SLOTS
    target = (group_of * GROUP_ROWS + offset[:, None] + ordinal).reshape(-1).astype(jnp.int32)

    def one_block(rows):
        gate = jnp.dot(rows, gate_weight, preferred_element_type=jnp.float32)
        up = jnp.dot(rows, up_weight, preferred_element_type=jnp.float32)
        return (jax.nn.silu(gate) * up).astype(jnp.bfloat16)

    computed = lax.map(one_block, tokens.reshape(blocks, ROWS_DEV, D)).reshape(ROWS, HID)
    hidden = jnp.zeros((N_BATCH * GROUP_ROWS, HID), jnp.bfloat16)
    return hidden.at[target].set(computed)
```

```python
import jax
import jax.numpy as jnp
from jax import lax
from jax.sharding import PartitionSpec as P


def place_rows(source, group_of, slots, groups_total):
    onehot = (group_of[:, None] == jnp.arange(groups_total, dtype=jnp.int32)[None, :]).astype(
        jnp.int32
    )
    ordinal = jnp.sum((jnp.cumsum(onehot, axis=0) - onehot) * onehot, axis=1)
    target = group_of * slots + ordinal
    chooser = (
        target[:, None] == jnp.arange(groups_total * slots, dtype=jnp.int32)[None, :]
    ).astype(jnp.bfloat16)
    placed = lax.dot_general(
        chooser, source, (((0,), (0,)), ((), ())), preferred_element_type=jnp.float32
    )
    return placed.astype(jnp.bfloat16)


def per_device(tokens, routes, gate_weight, up_weight):
    row_count = tokens.shape[0]
    hid = gate_weight.shape[1]
    groups_total = lax.axis_size("batch")
    wx_count = lax.axis_size("wx")
    slots = 2 * row_count // groups_total
    gathered = lax.all_gather(tokens, "wx", axis=0, tiled=True)
    group_all = lax.all_gather(routes, "wx", axis=0, tiled=True)
    gate = jnp.dot(gathered, gate_weight, preferred_element_type=jnp.float32)
    up = jnp.dot(gathered, up_weight, preferred_element_type=jnp.float32)
    both = jnp.concatenate([gate, up], axis=1)
    summed = lax.psum_scatter(both, "wy", scatter_dimension=0, tiled=True)
    gate_sum, up_sum = summed[:, :hid], summed[:, hid:]
    hidden = (jax.nn.silu(gate_sum) * up_sum).astype(jnp.bfloat16)
    own = lax.axis_index("wy")
    group_of = lax.dynamic_slice_in_dim(group_all.reshape(wx_count, row_count), own, 1, 0)[0]
    placed = place_rows(hidden, group_of, slots, groups_total)
    placed = placed.reshape(groups_total, slots, hid)
    arrived = lax.all_to_all(placed, "batch", split_axis=0, concat_axis=0, tiled=True)
    return arrived.reshape(groups_total * slots, hid)


def solution(mesh):
    placed = (P(("batch", "wx"), "wy"), P(("batch", "wx"), None), P("wy", "wx"), P("wy", "wx"))
    return jax.shard_map(
        per_device, mesh=mesh, in_specs=placed, out_specs=P(("batch", "wy"), "wx"), check_vma=False
    )
```

```python
import jax
import jax.numpy as jnp
from jax import lax
from jax.sharding import PartitionSpec as P


def place_rows(source, group_of, slots, groups_total):
    onehot = (group_of[:, None] == jnp.arange(groups_total, dtype=jnp.int32)[None, :]).astype(
        jnp.int32
    )
    ordinal = jnp.sum((jnp.cumsum(onehot, axis=0) - onehot) * onehot, axis=1)
    target = group_of * slots + ordinal
    chooser = (
        target[:, None] == jnp.arange(groups_total * slots, dtype=jnp.int32)[None, :]
    ).astype(jnp.bfloat16)
    placed = lax.dot_general(
        chooser, source, (((0,), (0,)), ((), ())), preferred_element_type=jnp.float32
    )
    return placed.astype(jnp.bfloat16)


def shift(value, axis, count, step):
    return lax.ppermute(value, axis, [(i, (i + step) % count) for i in range(count)])


def per_device(tokens, routes, gate_weight, up_weight):
    row_count = tokens.shape[0]
    hid = gate_weight.shape[1]
    groups_total = lax.axis_size("batch")
    nx = lax.axis_size("wx")
    ny = lax.axis_size("wy")
    assert nx == 4 and ny == 4
    slots = 2 * row_count // groups_total
    half = row_count // 2
    x = lax.axis_index("wx")
    y = lax.axis_index("wy")

    pairs = [(w * ny + v, v * ny + w) for w in range(nx) for v in range(ny)]
    group_of = lax.ppermute(routes, ("wx", "wy"), pairs)[:, 0]

    def partial(rows):
        gate = jnp.dot(rows, gate_weight, preferred_element_type=jnp.float32)
        up = jnp.dot(rows, up_weight, preferred_element_type=jnp.float32)
        return jnp.concatenate([gate, up], axis=1)

    from_left = shift(tokens, "wx", nx, 1)
    from_right = shift(tokens, "wx", nx, -1)
    part_own = partial(tokens)
    far_a = shift(from_left[:half], "wx", nx, 1)
    far_b = shift(from_right[half:], "wx", nx, -1)
    part_left = partial(from_left)
    part_right = partial(from_right)
    part_far = jnp.concatenate([partial(far_a), partial(far_b)], axis=0)
    parts = jnp.stack([part_own, part_right, part_far, part_left])

    total = lax.dynamic_index_in_dim(parts, (y - x) % nx, 0, keepdims=False)
    for d in (1, 2, 3):
        send = lax.dynamic_index_in_dim(parts, (y + d - x) % nx, 0, keepdims=False)
        total = total + shift(send, "wy", ny, d)
    gate_sum, up_sum = total[:, :hid], total[:, hid:]
    hidden = (jax.nn.silu(gate_sum) * up_sum).astype(jnp.bfloat16)
    placed = place_rows(hidden, group_of, slots, groups_total)
    placed = placed.reshape(groups_total, slots, hid)
    arrived = lax.all_to_all(placed, "batch", split_axis=0, concat_axis=0, tiled=True)
    return arrived.reshape(groups_total * slots, hid)


def solution(mesh):
    placed = (P(("batch", "wx"), "wy"), P(("batch", "wx"), None), P("wy", "wx"), P("wy", "wx"))
    return jax.shard_map(
        per_device, mesh=mesh, in_specs=placed, out_specs=P(("batch", "wy"), "wx"), check_vma=False
    )
```

```python
import jax
import jax.numpy as jnp
from jax import lax
from jax.sharding import PartitionSpec as P


def place_rows(source, group_of, slots, groups_total):
    onehot = (group_of[:, None] == jnp.arange(groups_total, dtype=jnp.int32)[None, :]).astype(
        jnp.int32
    )
    ordinal = jnp.sum((jnp.cumsum(onehot, axis=0) - onehot) * onehot, axis=1)
    target = group_of * slots + ordinal
    chooser = (
        target[:, None] == jnp.arange(groups_total * slots, dtype=jnp.int32)[None, :]
    ).astype(jnp.bfloat16)
    placed = lax.dot_general(
        chooser, source, (((0,), (0,)), ((), ())), preferred_element_type=jnp.float32
    )
    return placed.astype(jnp.bfloat16)


def shift(value, axis, count, step):
    return lax.ppermute(value, axis, [(i, (i + step) % count) for i in range(count)])


def per_device(tokens, routes, gate_weight, up_weight):
    row_count = tokens.shape[0]
    hid = gate_weight.shape[1]
    groups_total = lax.axis_size("batch")
    nx = lax.axis_size("wx")
    ny = lax.axis_size("wy")
    assert nx == 4 and ny == 4
    slots = 2 * row_count // groups_total
    half = row_count // 2
    quarter = hid // ny
    x = lax.axis_index("wx")
    y = lax.axis_index("wy")

    pairs = [(w * ny + v, v * ny + w) for w in range(nx) for v in range(ny)]
    group_of = lax.ppermute(routes, ("wx", "wy"), pairs)[:, 0]

    w_all = jnp.concatenate(
        [m[:, j * quarter:(j + 1) * quarter] for j in range(ny) for m in (gate_weight, up_weight)],
        axis=1,
    )

    def partial(rows):
        out = jnp.dot(rows, w_all, preferred_element_type=jnp.float32)
        return out.reshape(rows.shape[0], ny, 2 * quarter).transpose(1, 0, 2)

    def reduce(parts):
        total = lax.dynamic_index_in_dim(parts, y, 0, keepdims=False)
        for d in range(1, ny):
            send = lax.dynamic_index_in_dim(parts, (y + d) % ny, 0, keepdims=False)
            total = total + shift(send, "wy", ny, d)
        return total

    from_left = shift(tokens, "wx", nx, 1)
    from_right = shift(tokens, "wx", nx, -1)
    sum_own = reduce(partial(tokens))
    far_a = shift(from_left[:half], "wx", nx, 1)
    far_b = shift(from_right[half:], "wx", nx, -1)
    sum_sides = reduce(jnp.concatenate([partial(from_left), partial(from_right)], axis=1))
    sum_far = reduce(jnp.concatenate([partial(far_a), partial(far_b)], axis=1))
    sums = jnp.stack([sum_own, sum_sides[row_count:], sum_far, sum_sides[:row_count]])
    hidden = (jax.nn.silu(sums[..., :quarter]) * sums[..., quarter:]).astype(jnp.bfloat16)

    got = [lax.dynamic_index_in_dim(hidden, (y - x) % nx, 0, keepdims=False)]
    for d in range(1, ny):
        send = lax.dynamic_index_in_dim(hidden, (y + d - x) % nx, 0, keepdims=False)
        got.append(shift(send, "wy", ny, d))
    by_shift = jnp.stack(got)
    quarters = jnp.take(by_shift, (y - jnp.arange(ny)) % ny, axis=0)
    block = quarters.transpose(1, 0, 2).reshape(row_count, hid)

    placed = place_rows(block, group_of, slots, groups_total)
    placed = placed.reshape(groups_total, slots, hid)
    arrived = lax.all_to_all(placed, "batch", split_axis=0, concat_axis=0, tiled=True)
    return arrived.reshape(groups_total * slots, hid)


def solution(mesh):
    placed = (P(("batch", "wx"), "wy"), P(("batch", "wx"), None), P("wy", "wx"), P("wy", "wx"))
    return jax.shard_map(
        per_device, mesh=mesh, in_specs=placed, out_specs=P(("batch", "wy"), "wx"), check_vma=False
    )
```

```python
import jax
import jax.numpy as jnp
from jax import lax
from jax.sharding import PartitionSpec as P


def place_rows(source, group_of, slots, groups_total):
    onehot = (group_of[:, None] == jnp.arange(groups_total, dtype=jnp.int32)[None, :]).astype(
        jnp.int32
    )
    ordinal = jnp.sum((jnp.cumsum(onehot, axis=0) - onehot) * onehot, axis=1)
    target = group_of * slots + ordinal
    chooser = (
        target[:, None] == jnp.arange(groups_total * slots, dtype=jnp.int32)[None, :]
    ).astype(jnp.bfloat16)
    placed = lax.dot_general(
        chooser, source, (((0,), (0,)), ((), ())), preferred_element_type=jnp.float32
    )
    return placed.astype(jnp.bfloat16)


def shift(value, axis, count, step):
    return lax.ppermute(value, axis, [(i, (i + step) % count) for i in range(count)])


def per_device(tokens, routes, gate_weight, up_weight):
    row_count = tokens.shape[0]
    hid = gate_weight.shape[1]
    groups_total = lax.axis_size("batch")
    nx = lax.axis_size("wx")
    ny = lax.axis_size("wy")
    assert nx == 4 and ny == 4
    slots = 2 * row_count // groups_total
    half = row_count // 2
    x = lax.axis_index("wx")
    y = lax.axis_index("wy")

    pairs = [(w * ny + v, v * ny + w) for w in range(nx) for v in range(ny)]
    group_of = lax.ppermute(routes, ("wx", "wy"), pairs)[:, 0]

    def partial(rows):
        gate = jnp.dot(rows, gate_weight, preferred_element_type=jnp.float32)
        up = jnp.dot(rows, up_weight, preferred_element_type=jnp.float32)
        return jnp.concatenate([gate, up], axis=1)

    def to_root(part, rel):
        got = []
        for d in range(1, ny):
            route = [(w * ny + (w + rel + d) % ny, w * ny + (w + rel) % ny) for w in range(nx)]
            got.append(lax.ppermute(part, ("wx", "wy"), route))
        mine = jnp.where((y - x) % nx == rel, part, jnp.zeros_like(part))
        return mine + got[0] + got[1] + got[2]

    from_left = shift(tokens, "wx", nx, 1)
    from_right = shift(tokens, "wx", nx, -1)
    total = to_root(partial(tokens), 0)
    far_a = shift(from_left[:half], "wx", nx, 1)
    far_b = shift(from_right[half:], "wx", nx, -1)
    total = total + to_root(partial(from_right), 1)
    total = total + to_root(partial(from_left), 3)
    far = jnp.concatenate([partial(far_a), partial(far_b)], axis=0)
    total = total + to_root(far, 2)

    gate_sum, up_sum = total[:, :hid], total[:, hid:]
    hidden = (jax.nn.silu(gate_sum) * up_sum).astype(jnp.bfloat16)
    placed = place_rows(hidden, group_of, slots, groups_total)
    placed = placed.reshape(groups_total, slots, hid)
    arrived = lax.all_to_all(placed, "batch", split_axis=0, concat_axis=0, tiled=True)
    return arrived.reshape(groups_total * slots, hid)


def solution(mesh):
    placed = (P(("batch", "wx"), "wy"), P(("batch", "wx"), None), P("wy", "wx"), P("wy", "wx"))
    return jax.shard_map(
        per_device, mesh=mesh, in_specs=placed, out_specs=P(("batch", "wy"), "wx"), check_vma=False
    )
```

```python
import jax
import jax.numpy as jnp
from jax import lax
from jax.sharding import Mesh, PartitionSpec as P


def place_rows(source, group_of, slots, groups_total):
    onehot = (group_of[:, None] == jnp.arange(groups_total, dtype=jnp.int32)[None, :]).astype(
        jnp.int32
    )
    ordinal = jnp.sum((jnp.cumsum(onehot, axis=0) - onehot) * onehot, axis=1)
    target = group_of * slots + ordinal
    chooser = (
        target[:, None] == jnp.arange(groups_total * slots, dtype=jnp.int32)[None, :]
    ).astype(jnp.bfloat16)
    placed = lax.dot_general(
        chooser, source, (((0,), (0,)), ((), ())), preferred_element_type=jnp.float32
    )
    return placed.astype(jnp.bfloat16)


def shift(value, axis, count, step):
    return lax.ppermute(value, axis, [(i, (i + step) % count) for i in range(count)])


def per_device(tokens, routes, gate_weight, up_weight):
    row_count = tokens.shape[0]
    hid = gate_weight.shape[1]
    chips = lax.axis_size("bz")
    cores = lax.axis_size("bc")
    groups_total = chips * cores
    nx = lax.axis_size("wx")
    ny = lax.axis_size("wy")
    assert nx == 4 and ny == 4
    slots = 2 * row_count // groups_total
    half = row_count // 2
    x = lax.axis_index("wx")
    y = lax.axis_index("wy")

    pairs = [(w * ny + v, v * ny + w) for w in range(nx) for v in range(ny)]
    group_of = lax.ppermute(routes, ("wx", "wy"), pairs)[:, 0]

    def partial(rows):
        gate = jnp.dot(rows, gate_weight, preferred_element_type=jnp.float32)
        up = jnp.dot(rows, up_weight, preferred_element_type=jnp.float32)
        return jnp.concatenate([gate, up], axis=1)

    from_left = shift(tokens, "wx", nx, 1)
    from_right = shift(tokens, "wx", nx, -1)
    part_own = partial(tokens)
    far_a = shift(from_left[:half], "wx", nx, 1)
    far_b = shift(from_right[half:], "wx", nx, -1)
    part_left = partial(from_left)
    part_right = partial(from_right)
    part_far = jnp.concatenate([partial(far_a), partial(far_b)], axis=0)
    parts = jnp.stack([part_own, part_right, part_far, part_left])

    total = lax.dynamic_index_in_dim(parts, (y - x) % nx, 0, keepdims=False)
    for d in (1, 2, 3):
        send = lax.dynamic_index_in_dim(parts, (y + d - x) % nx, 0, keepdims=False)
        total = total + shift(send, "wy", ny, d)
    gate_sum, up_sum = total[:, :hid], total[:, hid:]
    hidden = (jax.nn.silu(gate_sum) * up_sum).astype(jnp.bfloat16)
    placed = place_rows(hidden, group_of, slots, groups_total)
    placed = placed.reshape(chips, cores, slots, hid)
    placed = lax.all_to_all(placed, "bc", split_axis=1, concat_axis=1, tiled=True)
    arrived = lax.all_to_all(placed, "bz", split_axis=0, concat_axis=0, tiled=True)
    return arrived.reshape(groups_total * slots, hid)


def solution(mesh):
    n_batch, n_wx, n_wy = mesh.devices.shape
    split = Mesh(mesh.devices.reshape(n_batch // 2, 2, n_wx, n_wy), ("bz", "bc", "wx", "wy"))
    rows = ("bz", "bc", "wx")
    placed = (P(rows, "wy"), P(rows, None), P("wy", "wx"), P("wy", "wx"))
    return jax.shard_map(
        per_device, mesh=split, in_specs=placed, out_specs=P(("bz", "bc", "wy"), "wx"), check_vma=False
    )
```

```python
import jax
import jax.numpy as jnp
from jax import lax
from jax.sharding import PartitionSpec as P


def place_rows(source, group_of, slots, groups_total):
    onehot = (group_of[:, None] == jnp.arange(groups_total, dtype=jnp.int32)[None, :]).astype(
        jnp.int32
    )
    ordinal = jnp.sum((jnp.cumsum(onehot, axis=0) - onehot) * onehot, axis=1)
    target = group_of * slots + ordinal
    chooser = (
        target[:, None] == jnp.arange(groups_total * slots, dtype=jnp.int32)[None, :]
    ).astype(jnp.bfloat16)
    placed = lax.dot_general(
        chooser, source, (((0,), (0,)), ((), ())), preferred_element_type=jnp.float32
    )
    return placed.astype(jnp.bfloat16)


def shift(value, axis, count, step):
    return lax.ppermute(value, axis, [(i, (i + step) % count) for i in range(count)])


def per_device(tokens, routes, gate_weight, up_weight):
    row_count = tokens.shape[0]
    hid = gate_weight.shape[1]
    groups_total = lax.axis_size("batch")
    nx = lax.axis_size("wx")
    ny = lax.axis_size("wy")
    assert nx == 4 and ny == 4
    slots = 2 * row_count // groups_total
    half = row_count // 2
    x = lax.axis_index("wx")
    y = lax.axis_index("wy")

    pairs = [(w * ny + v, v * ny + w) for w in range(nx) for v in range(ny)]
    group_of = lax.ppermute(routes, ("wx", "wy"), pairs)[:, 0]

    def partial(rows):
        gate = jnp.dot(rows, gate_weight, preferred_element_type=jnp.float32)
        up = jnp.dot(rows, up_weight, preferred_element_type=jnp.float32)
        return jnp.concatenate([gate, up], axis=1)

    from_left = shift(tokens, "wx", nx, 1)
    from_right = shift(tokens, "wx", nx, -1)
    part_own = partial(tokens)
    far_a = shift(from_left[:half], "wx", nx, 1)
    far_b = shift(from_right[half:], "wx", nx, -1)
    part_left = partial(from_left)
    part_right = partial(from_right)
    part_far = jnp.concatenate([partial(far_a), partial(far_b)], axis=0)
    parts = jnp.stack([part_own, part_right, part_far, part_left])

    def block(w):
        return lax.dynamic_index_in_dim(parts, (w - x) % nx, 0, keepdims=False)

    far_part = block(y + 2)
    via_right = shift(far_part[:half], "wy", ny, -1)
    via_left = shift(far_part[half:], "wy", ny, 1)
    to_left = block(y - 1)
    to_left = jnp.concatenate([to_left[:half] + via_right, to_left[half:]], axis=0)
    to_right = block(y + 1)
    to_right = jnp.concatenate([to_right[:half], to_right[half:] + via_left], axis=0)
    total = block(y) + shift(to_left, "wy", ny, -1) + shift(to_right, "wy", ny, 1)
    gate_sum, up_sum = total[:, :hid], total[:, hid:]
    hidden = (jax.nn.silu(gate_sum) * up_sum).astype(jnp.bfloat16)
    placed = place_rows(hidden, group_of, slots, groups_total)
    placed = placed.reshape(groups_total, slots, hid)
    arrived = lax.all_to_all(placed, "batch", split_axis=0, concat_axis=0, tiled=True)
    return arrived.reshape(groups_total * slots, hid)


def solution(mesh):
    placed = (P(("batch", "wx"), "wy"), P(("batch", "wx"), None), P("wy", "wx"), P("wy", "wx"))
    return jax.shard_map(
        per_device, mesh=mesh, in_specs=placed, out_specs=P(("batch", "wy"), "wx"), check_vma=False
    )
```

```python
import jax
import jax.numpy as jnp
from jax import lax
from jax.sharding import PartitionSpec as P


def place_rows(source, group_of, slots, groups_total):
    onehot = (group_of[:, None] == jnp.arange(groups_total, dtype=jnp.int32)[None, :]).astype(
        jnp.int32
    )
    ordinal = jnp.sum((jnp.cumsum(onehot, axis=0) - onehot) * onehot, axis=1)
    target = group_of * slots + ordinal
    chooser = (
        target[:, None] == jnp.arange(groups_total * slots, dtype=jnp.int32)[None, :]
    ).astype(jnp.bfloat16)
    placed = lax.dot_general(
        chooser, source, (((0,), (0,)), ((), ())), preferred_element_type=jnp.float32
    )
    return placed.astype(jnp.bfloat16)


def shift(value, axis, count, step):
    return lax.ppermute(value, axis, [(i, (i + step) % count) for i in range(count)])


def per_device(tokens, routes, gate_weight, up_weight):
    row_count = tokens.shape[0]
    hid = gate_weight.shape[1]
    groups_total = lax.axis_size("batch")
    nx = lax.axis_size("wx")
    ny = lax.axis_size("wy")
    assert nx == 4 and ny == 4
    slots = 2 * row_count // groups_total
    half = row_count // 2
    x = lax.axis_index("wx")
    y = lax.axis_index("wy")

    pairs = [(w * ny + v, v * ny + w) for w in range(nx) for v in range(ny)]
    group_of = lax.ppermute(routes, ("wx", "wy"), pairs)[:, 0]

    def partial(rows):
        gate = jnp.dot(rows, gate_weight, preferred_element_type=jnp.float32)
        up = jnp.dot(rows, up_weight, preferred_element_type=jnp.float32)
        return jnp.concatenate([gate, up], axis=1)

    def gather(own):
        cut = own.shape[0] // 2
        from_left = shift(own, "wx", nx, 1)
        from_right = shift(own, "wx", nx, -1)
        far_a = shift(from_left[:cut], "wx", nx, 1)
        far_b = shift(from_right[cut:], "wx", nx, -1)
        return from_left, from_right, far_a, far_b

    def feature_sum(own, from_left, from_right, far_a, far_b):
        far = jnp.concatenate([partial(far_a), partial(far_b)], axis=0)
        parts = jnp.stack([partial(own), partial(from_right), far, partial(from_left)])
        cut = own.shape[0] // 2

        def block(w):
            return lax.dynamic_index_in_dim(parts, (w - x) % nx, 0, keepdims=False)

        far_part = block(y + 2)
        via_right = shift(far_part[:cut], "wy", ny, -1)
        via_left = shift(far_part[cut:], "wy", ny, 1)
        to_left = block(y - 1)
        to_left = jnp.concatenate([to_left[:cut] + via_right, to_left[cut:]], axis=0)
        to_right = block(y + 1)
        to_right = jnp.concatenate([to_right[:cut], to_right[cut:] + via_left], axis=0)
        return block(y) + shift(to_left, "wy", ny, -1) + shift(to_right, "wy", ny, 1)

    first, second = tokens[:half], tokens[half:]
    got_first = gather(first)
    second, _ = lax.optimization_barrier((second, got_first[:2]))
    got_second = gather(second)
    total = jnp.concatenate(
        [feature_sum(first, *got_first), feature_sum(second, *got_second)], axis=0
    )
    gate_sum, up_sum = total[:, :hid], total[:, hid:]
    hidden = (jax.nn.silu(gate_sum) * up_sum).astype(jnp.bfloat16)
    placed = place_rows(hidden, group_of, slots, groups_total)
    placed = placed.reshape(groups_total, slots, hid)
    arrived = lax.all_to_all(placed, "batch", split_axis=0, concat_axis=0, tiled=True)
    return arrived.reshape(groups_total * slots, hid)


def solution(mesh):
    placed = (P(("batch", "wx"), "wy"), P(("batch", "wx"), None), P("wy", "wx"), P("wy", "wx"))
    return jax.shard_map(
        per_device, mesh=mesh, in_specs=placed, out_specs=P(("batch", "wy"), "wx"), check_vma=False
    )
```

```python
import jax
import jax.numpy as jnp
from jax import lax
from jax.sharding import PartitionSpec as P


def place_rows(source, group_of, slots, groups_total):
    onehot = (group_of[:, None] == jnp.arange(groups_total, dtype=jnp.int32)[None, :]).astype(
        jnp.int32
    )
    ordinal = jnp.sum((jnp.cumsum(onehot, axis=0) - onehot) * onehot, axis=1)
    target = group_of * slots + ordinal
    chooser = (
        target[:, None] == jnp.arange(groups_total * slots, dtype=jnp.int32)[None, :]
    ).astype(jnp.bfloat16)
    placed = lax.dot_general(
        chooser, source, (((0,), (0,)), ((), ())), preferred_element_type=jnp.float32
    )
    return placed.astype(jnp.bfloat16)


def shift(value, axis, count, step):
    return lax.ppermute(value, axis, [(i, (i + step) % count) for i in range(count)])


def per_device(tokens, routes, gate_weight, up_weight):
    row_count = tokens.shape[0]
    hid = gate_weight.shape[1]
    groups_total = lax.axis_size("batch")
    nx = lax.axis_size("wx")
    ny = lax.axis_size("wy")
    assert nx == 4 and ny == 4
    slots = 2 * row_count // groups_total
    half = row_count // 2
    x = lax.axis_index("wx")
    y = lax.axis_index("wy")

    pairs = [(w * ny + v, v * ny + w) for w in range(nx) for v in range(ny)]
    group_of = lax.ppermute(routes, ("wx", "wy"), pairs)[:, 0]

    def partial(rows):
        gate = jnp.dot(rows, gate_weight, preferred_element_type=jnp.float32)
        up = jnp.dot(rows, up_weight, preferred_element_type=jnp.float32)
        return jnp.concatenate([gate, up], axis=1)

    from_left = shift(tokens, "wx", nx, 1)
    from_right = shift(tokens, "wx", nx, -1)
    part_own = partial(tokens)
    far_a = shift(from_left[:half], "wx", nx, 1)
    far_b = shift(from_right[half:], "wx", nx, -1)
    part_left = partial(from_left)
    part_right = partial(from_right)
    part_far = jnp.concatenate([partial(far_a), partial(far_b)], axis=0)
    parts = jnp.stack([part_own, part_right, part_far, part_left])

    def block(w):
        return lax.dynamic_index_in_dim(parts, (w - x) % nx, 0, keepdims=False)

    far_part = block(y + 2)
    via_right = shift(far_part[:half], "wy", ny, -1)
    via_left = shift(far_part[half:], "wy", ny, 1)
    to_left = block(y - 1)
    to_left = jnp.concatenate([to_left[:half] + via_right, to_left[half:]], axis=0)
    to_right = block(y + 1)
    to_right = jnp.concatenate([to_right[:half], to_right[half:] + via_left], axis=0)
    total = block(y) + shift(to_left, "wy", ny, -1) + shift(to_right, "wy", ny, 1)
    gate_sum, up_sum = total[:, :hid], total[:, hid:]
    hidden = (jax.nn.silu(gate_sum) * up_sum).astype(jnp.bfloat16)
    placed = place_rows(hidden, group_of, slots, groups_total)
    placed = placed.reshape(groups_total, slots, hid)
    b = lax.axis_index("batch")
    got = [lax.dynamic_index_in_dim(placed, b, 0, keepdims=False)]
    for s in range(1, groups_total):
        send = lax.dynamic_index_in_dim(placed, (b + s) % groups_total, 0, keepdims=False)
        got.append(shift(send, "batch", groups_total, s))
    by_shift = jnp.stack(got)
    arrived = jnp.take(by_shift, (b - jnp.arange(groups_total)) % groups_total, axis=0)
    return arrived.reshape(groups_total * slots, hid)


def solution(mesh):
    placed = (P(("batch", "wx"), "wy"), P(("batch", "wx"), None), P("wy", "wx"), P("wy", "wx"))
    return jax.shard_map(
        per_device, mesh=mesh, in_specs=placed, out_specs=P(("batch", "wy"), "wx"), check_vma=False
    )
```

```python
import jax
import jax.numpy as jnp
from jax import lax
from jax.sharding import PartitionSpec as P


def place_rows(source, group_of, slots, groups_total):
    onehot = (group_of[:, None] == jnp.arange(groups_total, dtype=jnp.int32)[None, :]).astype(
        jnp.int32
    )
    ordinal = jnp.sum((jnp.cumsum(onehot, axis=0) - onehot) * onehot, axis=1)
    target = group_of * slots + ordinal
    chooser = (
        target[:, None] == jnp.arange(groups_total * slots, dtype=jnp.int32)[None, :]
    ).astype(jnp.bfloat16)
    placed = lax.dot_general(
        chooser, source, (((0,), (0,)), ((), ())), preferred_element_type=jnp.float32
    )
    return placed.astype(jnp.bfloat16)


def shift(value, axis, count, step):
    return lax.ppermute(value, axis, [(i, (i + step) % count) for i in range(count)])


def per_device(tokens, routes, gate_weight, up_weight):
    row_count = tokens.shape[0]
    hid = gate_weight.shape[1]
    groups_total = lax.axis_size("batch")
    nx = lax.axis_size("wx")
    ny = lax.axis_size("wy")
    assert nx == 4 and ny == 4
    slots = 2 * row_count // groups_total
    half = row_count // 2
    x = lax.axis_index("wx")
    y = lax.axis_index("wy")

    pairs = [(w * ny + v, v * ny + w) for w in range(nx) for v in range(ny)]
    group_of = lax.ppermute(routes, ("wx", "wy"), pairs)[:, 0]

    def partial(rows):
        gate = jnp.dot(rows, gate_weight, preferred_element_type=jnp.float32)
        up = jnp.dot(rows, up_weight, preferred_element_type=jnp.float32)
        return jnp.concatenate([gate, up], axis=1)

    from_left = shift(tokens, "wx", nx, 1)
    from_right = shift(tokens, "wx", nx, -1)
    part_own = partial(tokens)
    far_a = shift(from_left[:half], "wx", nx, 1)
    far_b = shift(from_right[half:], "wx", nx, -1)
    part_left = partial(from_left)
    part_right = partial(from_right)

    near = jnp.stack([part_own, part_right, part_own, part_left])
    total = jnp.zeros_like(part_own)
    for d in range(1, ny):
        route = [
            (w * ny + v, w * ny + (v + d) % ny)
            for w in range(nx)
            for v in range(ny)
            if (v + d) % ny != (w + 2) % ny
        ]
        send = lax.dynamic_index_in_dim(near, (y + d - x) % nx, 0, keepdims=False)
        total = total + lax.ppermute(send, ("wx", "wy"), route)
    part_far = jnp.concatenate([partial(far_a), partial(far_b)], axis=0)
    for d in range(1, ny):
        route = [(w * ny + (w + 2 - d) % ny, w * ny + (w + 2) % ny) for w in range(nx)]
        total = total + lax.ppermute(part_far, ("wx", "wy"), route)
    parts = jnp.stack([part_own, part_right, part_far, part_left])
    total = total + lax.dynamic_index_in_dim(parts, (y - x) % nx, 0, keepdims=False)
    gate_sum, up_sum = total[:, :hid], total[:, hid:]
    hidden = (jax.nn.silu(gate_sum) * up_sum).astype(jnp.bfloat16)
    placed = place_rows(hidden, group_of, slots, groups_total)
    placed = placed.reshape(groups_total, slots, hid)
    arrived = lax.all_to_all(placed, "batch", split_axis=0, concat_axis=0, tiled=True)
    return arrived.reshape(groups_total * slots, hid)


def solution(mesh):
    placed = (P(("batch", "wx"), "wy"), P(("batch", "wx"), None), P("wy", "wx"), P("wy", "wx"))
    return jax.shard_map(
        per_device, mesh=mesh, in_specs=placed, out_specs=P(("batch", "wy"), "wx"), check_vma=False
    )
```

```python
import jax
import jax.numpy as jnp
from jax import lax
from jax.sharding import PartitionSpec as P


def place_rows(source, group_of, slots, groups_total):
    onehot = (group_of[:, None] == jnp.arange(groups_total, dtype=jnp.int32)[None, :]).astype(
        jnp.int32
    )
    ordinal = jnp.sum((jnp.cumsum(onehot, axis=0) - onehot) * onehot, axis=1)
    target = group_of * slots + ordinal
    chooser = (
        target[:, None] == jnp.arange(groups_total * slots, dtype=jnp.int32)[None, :]
    ).astype(jnp.bfloat16)
    placed = lax.dot_general(
        chooser, source, (((0,), (0,)), ((), ())), preferred_element_type=jnp.float32
    )
    return placed.astype(jnp.bfloat16)


def shift(value, axis, count, step):
    return lax.ppermute(value, axis, [(i, (i + step) % count) for i in range(count)])


def per_device(tokens, routes, gate_weight, up_weight):
    row_count = tokens.shape[0]
    hid = gate_weight.shape[1]
    groups_total = lax.axis_size("batch")
    nx = lax.axis_size("wx")
    ny = lax.axis_size("wy")
    assert nx == 4 and ny == 4
    slots = 2 * row_count // groups_total
    half = row_count // 2
    x = lax.axis_index("wx")
    y = lax.axis_index("wy")

    pairs = [(w * ny + v, v * ny + w) for w in range(nx) for v in range(ny)]
    group_of = lax.ppermute(routes, ("wx", "wy"), pairs)[:, 0]

    def partial(rows):
        gate = jnp.dot(rows, gate_weight, preferred_element_type=jnp.float32)
        up = jnp.dot(rows, up_weight, preferred_element_type=jnp.float32)
        return jnp.concatenate([gate, up], axis=1)

    from_left = shift(tokens, "wx", nx, 1)
    from_right = shift(tokens, "wx", nx, -1)
    part_own = partial(tokens)
    far_a = shift(from_left[:half], "wx", nx, 1)
    far_b = shift(from_right[half:], "wx", nx, -1)
    part_left = partial(from_left)
    part_right = partial(from_right)
    part_far = partial(jnp.concatenate([far_a, far_b], axis=0))
    parts = jnp.stack([part_own, part_right, part_far, part_left])

    def block(w):
        return lax.dynamic_index_in_dim(parts, (w - x) % nx, 0, keepdims=False)

    far_part = block(y + 2)
    via_right = shift(far_part[:half], "wy", ny, -1)
    via_left = shift(far_part[half:], "wy", ny, 1)
    to_left = block(y - 1).at[:half].add(via_right)
    to_right = block(y + 1).at[half:].add(via_left)
    total = block(y) + shift(to_left, "wy", ny, -1) + shift(to_right, "wy", ny, 1)
    gate_sum, up_sum = total[:, :hid], total[:, hid:]
    hidden = (jax.nn.silu(gate_sum) * up_sum).astype(jnp.bfloat16)
    placed = place_rows(hidden, group_of, slots, groups_total)
    placed = placed.reshape(groups_total, slots, hid)
    arrived = lax.all_to_all(placed, "batch", split_axis=0, concat_axis=0, tiled=True)
    return arrived.reshape(groups_total * slots, hid)


def solution(mesh):
    placed = (P(("batch", "wx"), "wy"), P(("batch", "wx"), None), P("wy", "wx"), P("wy", "wx"))
    return jax.shard_map(
        per_device, mesh=mesh, in_specs=placed, out_specs=P(("batch", "wy"), "wx"), check_vma=False
    )
```

```python
import jax
import jax.numpy as jnp
from jax import lax
from jax.sharding import PartitionSpec as P


def place_rows(source, group_of, slots, groups_total):
    onehot = (group_of[:, None] == jnp.arange(groups_total, dtype=jnp.int32)[None, :]).astype(
        jnp.int32
    )
    ordinal = jnp.sum((jnp.cumsum(onehot, axis=0) - onehot) * onehot, axis=1)
    target = group_of * slots + ordinal
    chooser = (
        target[:, None] == jnp.arange(groups_total * slots, dtype=jnp.int32)[None, :]
    ).astype(jnp.bfloat16)
    placed = lax.dot_general(
        chooser, source, (((0,), (0,)), ((), ())), preferred_element_type=jnp.float32
    )
    return placed.astype(jnp.bfloat16)


def shift(value, axis, count, step):
    return lax.ppermute(value, axis, [(i, (i + step) % count) for i in range(count)])


def per_device(tokens, routes, gate_weight, up_weight):
    row_count = tokens.shape[0]
    hid = gate_weight.shape[1]
    groups_total = lax.axis_size("batch")
    nx = lax.axis_size("wx")
    ny = lax.axis_size("wy")
    assert nx == 4 and ny == 4
    slots = 2 * row_count // groups_total
    half = row_count // 2
    x = lax.axis_index("wx")
    y = lax.axis_index("wy")

    pairs = [(w * ny + v, v * ny + w) for w in range(nx) for v in range(ny)]
    group_of = lax.ppermute(routes, ("wx", "wy"), pairs)[:, 0]

    def partial(rows):
        gate = jnp.dot(rows, gate_weight, preferred_element_type=jnp.float32)
        up = jnp.dot(rows, up_weight, preferred_element_type=jnp.float32)
        return jnp.concatenate([gate, up], axis=1)

    from_left = shift(tokens, "wx", nx, 1)
    from_right = shift(tokens, "wx", nx, -1)
    part_own = partial(tokens)
    far_a = shift(from_left[:half], "wx", nx, 1)
    far_b = shift(from_right[half:], "wx", nx, -1)
    part_left = partial(from_left)
    part_right = partial(from_right)
    part_far = partial(jnp.concatenate([far_a, far_b], axis=0))
    parts = jnp.stack([part_own, part_right, part_far, part_left])
    near = jnp.stack([part_own, part_right, part_own, part_left])

    def block(w):
        return lax.dynamic_index_in_dim(parts, (w - x) % nx, 0, keepdims=False)

    opposite = lax.dynamic_index_in_dim(near, (y + 2 - x) % nx, 0, keepdims=False)
    via_right = shift(opposite[:half], "wy", ny, -1)
    via_left = shift(opposite[half:], "wy", ny, 1)
    via_right = jnp.where((y + 1 - x) % ny == 0, jnp.zeros_like(via_right), via_right)
    via_left = jnp.where((y - 1 - x) % ny == 0, jnp.zeros_like(via_left), via_left)
    across = lax.ppermute(part_far, ("wx", "wy"), [(w * ny + w, w * ny + (w + 2) % ny) for w in range(nx)])
    to_left = block(y - 1).at[:half].add(via_right)
    to_right = block(y + 1).at[half:].add(via_left)
    total = block(y) + shift(to_left, "wy", ny, -1) + shift(to_right, "wy", ny, 1) + across
    gate_sum, up_sum = total[:, :hid], total[:, hid:]
    hidden = (jax.nn.silu(gate_sum) * up_sum).astype(jnp.bfloat16)
    placed = place_rows(hidden, group_of, slots, groups_total)
    placed = placed.reshape(groups_total, slots, hid)
    arrived = lax.all_to_all(placed, "batch", split_axis=0, concat_axis=0, tiled=True)
    return arrived.reshape(groups_total * slots, hid)


def solution(mesh):
    placed = (P(("batch", "wx"), "wy"), P(("batch", "wx"), None), P("wy", "wx"), P("wy", "wx"))
    return jax.shard_map(
        per_device, mesh=mesh, in_specs=placed, out_specs=P(("batch", "wy"), "wx"), check_vma=False
    )
```

```python
import jax
import jax.numpy as jnp
from jax import lax
from jax.sharding import PartitionSpec as P


def place_rows(source, group_of, slots, groups_total):
    onehot = (group_of[:, None] == jnp.arange(groups_total, dtype=jnp.int32)[None, :]).astype(
        jnp.int32
    )
    ordinal = jnp.sum((jnp.cumsum(onehot, axis=0) - onehot) * onehot, axis=1)
    target = group_of * slots + ordinal
    chooser = (
        target[:, None] == jnp.arange(groups_total * slots, dtype=jnp.int32)[None, :]
    ).astype(jnp.bfloat16)
    placed = lax.dot_general(
        chooser, source, (((0,), (0,)), ((), ())), preferred_element_type=jnp.float32
    )
    return placed.astype(jnp.bfloat16)


def shift(value, axis, count, step):
    return lax.ppermute(value, axis, [(i, (i + step) % count) for i in range(count)])


def per_device(tokens, routes, gate_weight, up_weight):
    row_count = tokens.shape[0]
    hid = gate_weight.shape[1]
    groups_total = lax.axis_size("batch")
    nx = lax.axis_size("wx")
    ny = lax.axis_size("wy")
    assert nx == 4 and ny == 4
    slots = 2 * row_count // groups_total
    half = row_count // 2
    x = lax.axis_index("wx")
    y = lax.axis_index("wy")

    pairs = [(w * ny + v, v * ny + w) for w in range(nx) for v in range(ny)]
    group_of = lax.ppermute(routes, ("wx", "wy"), pairs)[:, 0]

    def partial(rows):
        gate = jnp.dot(rows, gate_weight, preferred_element_type=jnp.float32)
        up = jnp.dot(rows, up_weight, preferred_element_type=jnp.float32)
        return jnp.concatenate([gate, up], axis=1)

    from_left = shift(tokens, "wx", nx, 1)
    from_right = shift(tokens, "wx", nx, -1)
    part_own = partial(tokens)
    far_a = shift(from_left[:half], "wx", nx, 1)
    far_b = shift(from_right[half:], "wx", nx, -1)
    part_left = partial(from_left)
    part_right = partial(from_right)
    part_far = partial(jnp.concatenate([far_a, far_b], axis=0))
    parts = jnp.stack([part_own, part_right, part_far, part_left])

    def block(w):
        return lax.dynamic_index_in_dim(parts, (w - x) % nx, 0, keepdims=False)

    far_part = block(y + 2)
    via_right = shift(far_part[:half], "wy", ny, -1)
    via_left = shift(far_part[half:], "wy", ny, 1)
    base_left, base_right = lax.optimization_barrier((block(y - 1), block(y + 1)))
    to_left = base_left.at[:half].add(via_right)
    to_right = base_right.at[half:].add(via_left)
    total = block(y) + shift(to_left, "wy", ny, -1) + shift(to_right, "wy", ny, 1)
    gate_sum, up_sum = total[:, :hid], total[:, hid:]
    hidden = (jax.nn.silu(gate_sum) * up_sum).astype(jnp.bfloat16)
    placed = place_rows(hidden, group_of, slots, groups_total)
    placed = placed.reshape(groups_total, slots, hid)
    arrived = lax.all_to_all(placed, "batch", split_axis=0, concat_axis=0, tiled=True)
    return arrived.reshape(groups_total * slots, hid)


def solution(mesh):
    placed = (P(("batch", "wx"), "wy"), P(("batch", "wx"), None), P("wy", "wx"), P("wy", "wx"))
    return jax.shard_map(
        per_device, mesh=mesh, in_specs=placed, out_specs=P(("batch", "wy"), "wx"), check_vma=False
    )
```

```python
import jax
import jax.numpy as jnp
from jax import lax
from jax.sharding import PartitionSpec as P


def place_rows(source, group_of, slots, groups_total):
    onehot = (group_of[:, None] == jnp.arange(groups_total, dtype=jnp.int32)[None, :]).astype(
        jnp.int32
    )
    ordinal = jnp.sum((jnp.cumsum(onehot, axis=0) - onehot) * onehot, axis=1)
    target = group_of * slots + ordinal
    chooser = (
        target[:, None] == jnp.arange(groups_total * slots, dtype=jnp.int32)[None, :]
    ).astype(jnp.bfloat16)
    placed = lax.dot_general(
        chooser, source, (((0,), (0,)), ((), ())), preferred_element_type=jnp.float32
    )
    return placed.astype(jnp.bfloat16)


def shift(value, axis, count, step):
    return lax.ppermute(value, axis, [(i, (i + step) % count) for i in range(count)])


def per_device(tokens, routes, gate_weight, up_weight):
    row_count = tokens.shape[0]
    hid = gate_weight.shape[1]
    groups_total = lax.axis_size("batch")
    nx = lax.axis_size("wx")
    ny = lax.axis_size("wy")
    assert nx == 4 and ny == 4
    slots = 2 * row_count // groups_total
    half = row_count // 2
    x = lax.axis_index("wx")
    y = lax.axis_index("wy")

    pairs = [(w * ny + v, v * ny + w) for w in range(nx) for v in range(ny)]
    group_of = lax.ppermute(routes, ("wx", "wy"), pairs)[:, 0]

    def partial(rows):
        gate = jnp.dot(rows, gate_weight, preferred_element_type=jnp.float32)
        up = jnp.dot(rows, up_weight, preferred_element_type=jnp.float32)
        return jnp.concatenate([gate, up], axis=1)

    left_a = shift(tokens[:half], "wx", nx, 1)
    right_b = shift(tokens[half:], "wx", nx, -1)
    part_own = partial(tokens)
    later, _ = lax.optimization_barrier((tokens, (left_a, right_b)))
    far_a = shift(left_a, "wx", nx, 1)
    far_b = shift(right_b, "wx", nx, -1)
    left_b = shift(later[half:], "wx", nx, 1)
    right_a = shift(later[:half], "wx", nx, -1)
    from_left = jnp.concatenate([left_a, left_b], axis=0)
    from_right = jnp.concatenate([right_a, right_b], axis=0)
    part_left = partial(from_left)
    part_right = partial(from_right)
    part_far = partial(jnp.concatenate([far_a, far_b], axis=0))
    parts = jnp.stack([part_own, part_right, part_far, part_left])

    def block(w):
        return lax.dynamic_index_in_dim(parts, (w - x) % nx, 0, keepdims=False)

    far_part = block(y + 2)
    via_right = shift(far_part[:half], "wy", ny, -1)
    via_left = shift(far_part[half:], "wy", ny, 1)
    to_left = block(y - 1).at[:half].add(via_right)
    to_right = block(y + 1).at[half:].add(via_left)
    total = block(y) + shift(to_left, "wy", ny, -1) + shift(to_right, "wy", ny, 1)
    gate_sum, up_sum = total[:, :hid], total[:, hid:]
    hidden = (jax.nn.silu(gate_sum) * up_sum).astype(jnp.bfloat16)
    placed = place_rows(hidden, group_of, slots, groups_total)
    placed = placed.reshape(groups_total, slots, hid)
    arrived = lax.all_to_all(placed, "batch", split_axis=0, concat_axis=0, tiled=True)
    return arrived.reshape(groups_total * slots, hid)


def solution(mesh):
    placed = (P(("batch", "wx"), "wy"), P(("batch", "wx"), None), P("wy", "wx"), P("wy", "wx"))
    return jax.shard_map(
        per_device, mesh=mesh, in_specs=placed, out_specs=P(("batch", "wy"), "wx"), check_vma=False
    )
```

```python
import jax
import jax.numpy as jnp
from jax import lax
from jax.sharding import PartitionSpec as P


def place_rows(source, group_of, slots, groups_total):
    onehot = (group_of[:, None] == jnp.arange(groups_total, dtype=jnp.int32)[None, :]).astype(
        jnp.int32
    )
    ordinal = jnp.sum((jnp.cumsum(onehot, axis=0) - onehot) * onehot, axis=1)
    target = group_of * slots + ordinal
    chooser = (
        target[:, None] == jnp.arange(groups_total * slots, dtype=jnp.int32)[None, :]
    ).astype(jnp.bfloat16)
    placed = lax.dot_general(
        chooser, source, (((0,), (0,)), ((), ())), preferred_element_type=jnp.float32
    )
    return placed.astype(jnp.bfloat16)


def shift(value, axis, count, step):
    return lax.ppermute(value, axis, [(i, (i + step) % count) for i in range(count)])


def per_device(tokens, routes, gate_weight, up_weight):
    row_count = tokens.shape[0]
    hid = gate_weight.shape[1]
    groups_total = lax.axis_size("batch")
    nx = lax.axis_size("wx")
    ny = lax.axis_size("wy")
    assert nx == 4 and ny == 4
    slots = 2 * row_count // groups_total
    half = row_count // 2
    x = lax.axis_index("wx")
    y = lax.axis_index("wy")

    pairs = [(w * ny + v, v * ny + w) for w in range(nx) for v in range(ny)]
    group_of = lax.ppermute(routes, ("wx", "wy"), pairs)[:, 0]

    both = jnp.concatenate([gate_weight, up_weight], axis=1)

    def partial(rows):
        return jnp.dot(rows, both, preferred_element_type=jnp.float32)

    from_left = shift(tokens, "wx", nx, 1)
    from_right = shift(tokens, "wx", nx, -1)
    part_own = partial(tokens)
    far_a = shift(from_left[:half], "wx", nx, 1)
    far_b = shift(from_right[half:], "wx", nx, -1)
    part_left = partial(from_left)
    part_right = partial(from_right)
    part_far = partial(jnp.concatenate([far_a, far_b], axis=0))
    parts = jnp.stack([part_own, part_right, part_far, part_left])

    def block(w):
        return lax.dynamic_index_in_dim(parts, (w - x) % nx, 0, keepdims=False)

    far_part = block(y + 2)
    via_right = shift(far_part[:half], "wy", ny, -1)
    via_left = shift(far_part[half:], "wy", ny, 1)
    to_left = block(y - 1).at[:half].add(via_right)
    to_right = block(y + 1).at[half:].add(via_left)
    total = block(y) + shift(to_left, "wy", ny, -1) + shift(to_right, "wy", ny, 1)
    gate_sum, up_sum = total[:, :hid], total[:, hid:]
    hidden = (jax.nn.silu(gate_sum) * up_sum).astype(jnp.bfloat16)
    placed = place_rows(hidden, group_of, slots, groups_total)
    placed = placed.reshape(groups_total, slots, hid)
    arrived = lax.all_to_all(placed, "batch", split_axis=0, concat_axis=0, tiled=True)
    return arrived.reshape(groups_total * slots, hid)


def solution(mesh):
    placed = (P(("batch", "wx"), "wy"), P(("batch", "wx"), None), P("wy", "wx"), P("wy", "wx"))
    return jax.shard_map(
        per_device, mesh=mesh, in_specs=placed, out_specs=P(("batch", "wy"), "wx"), check_vma=False
    )
```
